128 devices in a mesh: dp: 16 (over y, z_hi, core), mp: 8 (over x, z_lo).
Axes of the slice: x: 4, y: 4, z: 4 (z_hi: 2, z_lo: 2; z = z_hi * 2 + z_lo), core: 2. Of those that a mesh axis runs over, the one named last changes fastest.
Arguments:
- features: bfloat16 [8192, 8192], P('mp', 'dp'), may hold values from -6 to 6
- cotangent: bfloat16 [8192, 8192], P('mp', 'dp'), may hold values from -6 to 6
- block_perm: int32 [16, 512], P('mp'), may hold values from 0 to 511, each once within a row
- w_gate: bfloat16 [16, 512, 2048], P('mp'), may hold values from -0.25 to 0.25
- w_up: bfloat16 [16, 512, 2048], P('mp'), may hold values from -0.25 to 0.25
- w_down: bfloat16 [16, 2048, 512], P('mp'), may hold values from -0.125 to 0.125
Outputs:
- outputs: bfloat16 [8192, 8192], P('mp', 'dp')
- d_features: bfloat16 [8192, 8192], P('mp', 'dp')
- gate_grad: float32 [16, 512, 2048], P('mp', 'dp')
- up_grad: float32 [16, 512, 2048], P('mp', 'dp')
- down_grad: float32 [16, 2048, 512], P('mp', 'dp')
The draws below stay inside these ranges and needn't reach their ends.
Inputs may be any that keep to these rules, and one draw needn't show every extreme that they name: Each row of block_perm names every number below 512 exactly once.
All inputs are finite; a program needn't handle non-finite values.
Results may differ from the reference program's by a relative error of at most 0.012.
Values may be sent and summed in bfloat16 or wider, within the bound.
No kernel may reach another device: no remote copies, remote signals or barrier semaphores. Data moves between devices by JAX's collectives and lax.ppermute only.
A program may use at most 128 MiB of HBM per device.

```python
import jax
import jax.numpy as jnp
from jax import lax

NB = 16
BI = 512
BH = 2048
TOK_DEV = 512
PIECE = 32
D = 8192
TOKENS = 8192
N_DP = 16


def block_levels(key, shape, cuts, smallest, top_value):
    gain, own = 1.0, jax.random.fold_in(key, 6)
    for dim, parts in cuts:
        steps = jnp.exp(jax.random.uniform(jax.random.fold_in(own, dim), (parts,), jnp.float32, smallest / len(cuts), top_value / len(cuts)))
        gain = gain * jnp.repeat(steps, shape[dim] // parts).reshape([-1 if axis == dim else 1 for axis in range(len(shape))])
    return gain


def normal_values(key, shape, spread, limit, split=(), held_as=jnp.bfloat16):
    loudness = block_levels(key, shape, split, -0.22, 0.18) if split else 1.0
    result = jax.random.normal(key, shape, jnp.float32) * spread * loudness
    return jnp.minimum(jnp.maximum(result, -limit), limit).astype(held_as)


def setup_inputs(seed: int = 0) -> dict:
    streams_of = jax.random.split(jax.random.key(seed), 7)
    features = normal_values(streams_of[0], (D, TOKENS), 1.0, 6.0, ((0, 8), (1, 16)))
    cotangent = normal_values(streams_of[1], (D, TOKENS), 1.0, 6.0, ((0, 8), (1, 16)))
    block_perm = jax.vmap(lambda own: jax.random.permutation(own, BI))(jax.random.split(streams_of[2], NB)).reshape((NB, BI)).astype(jnp.int32)
    w_gate = normal_values(streams_of[3], (NB, BI, BH), BI ** -0.5, 0.25, ((0, 8),))
    w_up = normal_values(streams_of[4], (NB, BI, BH), BI ** -0.5, 0.25, ((0, 8),))
    w_down = normal_values(streams_of[5], (NB, BH, BI), BH ** -0.5, 0.125, ((0, 8),))
    return dict(features=features, cotangent=cotangent, block_perm=block_perm, w_gate=w_gate, w_up=w_up, w_down=w_down)


input_scale = 2.0
output_scale = 0.5


def rounded(value):
    return lax.optimization_barrier(value.astype(jnp.bfloat16)).astype(jnp.float32)


def one_block(operands):
    feat_block, cot_block, perm_row, gate_w, up_w, down_w = operands
    grad_scale = TOKENS ** -0.5
    feat_rows = feat_block.reshape(BI, TOKENS)
    cot_rows = cot_block.reshape(BI, TOKENS)
    places = jnp.arange(BI, dtype=jnp.int32)
    inverse = jnp.zeros((BI,), jnp.int32).at[perm_row.astype(jnp.int32)].set(places)
    gate_rows = gate_w[inverse]
    up_rows = up_w[inverse]
    gate = jnp.dot(feat_rows.T, gate_rows, preferred_element_type=jnp.float32) * input_scale
    up = jnp.dot(feat_rows.T, up_rows, preferred_element_type=jnp.float32) * input_scale
    sig = jax.nn.sigmoid(gate)
    act = gate * sig
    hidden = (act * up).astype(jnp.bfloat16)
    mixed = (jnp.dot(hidden, down_w, preferred_element_type=jnp.float32) * output_scale).astype(jnp.bfloat16)
    d_hidden = jnp.dot(cot_rows.T, down_w.T, preferred_element_type=jnp.float32) * output_scale
    d_gate = (d_hidden * up * (sig * (1.0 + gate * (1.0 - sig)))).astype(jnp.bfloat16)
    d_up = (d_hidden * act).astype(jnp.bfloat16)
    d_mixed = ((jnp.dot(d_gate, gate_rows.T, preferred_element_type=jnp.float32)
                + jnp.dot(d_up, up_rows.T, preferred_element_type=jnp.float32)) * input_scale).astype(jnp.bfloat16)
    hid_groups = hidden.astype(jnp.float32).reshape(N_DP, TOK_DEV, BH)
    cot_groups = cot_rows.astype(jnp.float32).reshape(BI, N_DP, TOK_DEV)
    feat_groups = feat_rows.astype(jnp.float32).reshape(BI, N_DP, TOK_DEV)
    dgate_groups = d_gate.astype(jnp.float32).reshape(N_DP, TOK_DEV, BH)
    dup_groups = d_up.astype(jnp.float32).reshape(N_DP, TOK_DEV, BH)
    down_part = jnp.einsum("gth,jgt->ghj", hid_groups, cot_groups) * (output_scale * grad_scale)
    gate_part = jnp.einsum("jgt,gth->gjh", feat_groups, dgate_groups) * (input_scale * grad_scale)
    up_part = jnp.einsum("jgt,gth->gjh", feat_groups, dup_groups) * (input_scale * grad_scale)
    gate_part = gate_part[:, perm_row.astype(jnp.int32), :]
    up_part = up_part[:, perm_row.astype(jnp.int32), :]
    down_grad = jnp.sum(rounded(down_part), axis=0)
    gate_grad = jnp.sum(rounded(gate_part), axis=0)
    up_grad = jnp.sum(rounded(up_part), axis=0)
    return mixed.T, d_mixed.T, gate_grad, up_grad, down_grad


def reference(features, cotangent, block_perm, w_gate, w_up, w_down):
    feat_view = features.reshape(NB, NB, PIECE, TOKENS).transpose(1, 0, 2, 3)
    cot_view = cotangent.reshape(NB, NB, PIECE, TOKENS).transpose(1, 0, 2, 3)
    mixed, d_mixed, gate_grad, up_grad, down_grad = lax.map(
        one_block, (feat_view, cot_view, block_perm, w_gate, w_up, w_down))
    outputs = mixed.reshape(NB, NB, PIECE, TOKENS).transpose(1, 0, 2, 3).reshape(D, TOKENS)
    d_features = d_mixed.reshape(NB, NB, PIECE, TOKENS).transpose(1, 0, 2, 3).reshape(D, TOKENS)
    return outputs, d_features, gate_grad, up_grad, down_grad
```

```python
import jax
import jax.numpy as jnp
from jax import lax
from jax.sharding import PartitionSpec as P

input_scale = 2.0
output_scale = 0.5


def perm_matrix(block_perm):
    count = block_perm.shape[1]
    targets = lax.broadcasted_iota(jnp.int32, (1, 1, count), 2)
    return (block_perm[:, :, None] == targets).astype(jnp.bfloat16)


def local(features, cotangent, block_perm, w_gate, w_up, w_down):
    tok_count = features.shape[1]
    blocks_here = w_gate.shape[0]
    inner = w_gate.shape[1]
    hidden_width = w_gate.shape[2]
    n_mp = lax.axis_size("mp")
    n_dp = lax.axis_size("dp")
    block_total = blocks_here * n_mp
    piece = inner // block_total
    s_here = features.shape[0] // (block_total * piece)
    grad_scale = (tok_count * n_dp) ** (-0.5)

    both = jnp.stack([features, cotangent]).reshape(2, s_here, block_total, piece, tok_count)
    both = lax.all_to_all(both, "mp", split_axis=2, concat_axis=1, tiled=True)
    feat_blocks = both[0]
    cot_blocks = both[1]

    onehot = perm_matrix(block_perm)
    feat_rows = feat_blocks.transpose(1, 0, 2, 3).reshape(blocks_here, inner, tok_count)
    feat_p = jnp.einsum(
        "bij,bjt->bit", onehot, feat_rows, preferred_element_type=jnp.float32
    ).astype(jnp.bfloat16)

    gate = (
        jnp.einsum("bit,bih->bth", feat_p, w_gate, preferred_element_type=jnp.float32)
        * input_scale
    )
    up = (
        jnp.einsum("bit,bih->bth", feat_p, w_up, preferred_element_type=jnp.float32)
        * input_scale
    )
    sig = jax.nn.sigmoid(gate)
    act = gate * sig
    hidden = (act * up).astype(jnp.bfloat16)
    down_view = w_down.reshape(blocks_here, hidden_width, block_total, piece)

    chunk = n_dp
    down_part = (
        jnp.einsum("bth,sbkt->bhsk", hidden, cot_blocks, preferred_element_type=jnp.float32)
        * (output_scale * grad_scale)
    ).astype(jnp.bfloat16)
    down_grad = lax.psum_scatter(
        down_part.reshape(blocks_here, hidden_width, inner), "dp", scatter_dimension=1, tiled=True
    ).astype(jnp.float32)

    mixed = (
        jnp.einsum("bth,bhsk->sbkt", hidden, down_view, preferred_element_type=jnp.float32)
        * output_scale
    ).astype(jnp.bfloat16)

    d_hidden = (
        jnp.einsum("sbkt,bhsk->bth", cot_blocks, down_view, preferred_element_type=jnp.float32)
        * output_scale
    )
    d_gate = (d_hidden * up * (sig * (1.0 + gate * (1.0 - sig)))).astype(jnp.bfloat16)
    d_up = (d_hidden * act).astype(jnp.bfloat16)

    gate_part = (
        jnp.einsum("bit,bth->bih", feat_p, d_gate, preferred_element_type=jnp.float32)
        * (input_scale * grad_scale)
    ).astype(jnp.bfloat16)
    up_part = (
        jnp.einsum("bit,bth->bih", feat_p, d_up, preferred_element_type=jnp.float32)
        * (input_scale * grad_scale)
    ).astype(jnp.bfloat16)
    gate_grad = lax.psum_scatter(gate_part, "dp", scatter_dimension=1, tiled=True).astype(
        jnp.float32
    )
    up_grad = lax.psum_scatter(up_part, "dp", scatter_dimension=1, tiled=True).astype(
        jnp.float32
    )

    d_mixed_p = (
        (
            jnp.einsum("bth,bih->bit", d_gate, w_gate, preferred_element_type=jnp.float32)
            + jnp.einsum("bth,bih->bit", d_up, w_up, preferred_element_type=jnp.float32)
        )
        * input_scale
    ).astype(jnp.bfloat16)
    d_mixed = jnp.einsum(
        "bij,bit->bjt", onehot, d_mixed_p, preferred_element_type=jnp.float32
    ).astype(jnp.bfloat16)
    d_mixed = d_mixed.reshape(blocks_here, block_total, piece, tok_count).transpose(1, 0, 2, 3)

    back = jnp.stack([mixed, d_mixed])
    back = lax.all_to_all(back, "mp", split_axis=1, concat_axis=2, tiled=True)
    outputs = back[0].reshape(features.shape)
    d_features = back[1].reshape(features.shape)
    del chunk
    return (outputs, d_features, gate_grad, up_grad, down_grad)


def solution(mesh):
    placed = (
        P("mp", "dp"),
        P("mp", "dp"),
        P("mp", None),
        P("mp", None, None),
        P("mp", None, None),
        P("mp", None, None),
    )
    return jax.shard_map(
        local,
        mesh=mesh,
        in_specs=placed,
        out_specs=(
            P("mp", "dp"),
            P("mp", "dp"),
            P("mp", "dp", None),
            P("mp", "dp", None),
            P("mp", "dp", None),
        ),
        check_vma=False,
    )
```

```python
import jax
import jax.numpy as jnp
from jax import lax
from jax.sharding import Mesh
from jax.sharding import PartitionSpec as P

input_scale = 2.0
output_scale = 0.5


def perm_matrix(block_perm):
    count = block_perm.shape[1]
    targets = lax.broadcasted_iota(jnp.int32, (1, 1, count), 2)
    return (block_perm[:, :, None] == targets).astype(jnp.bfloat16)


def reduce_rows(part):
    blocks, rows, cols = part.shape
    n_chip = lax.axis_size("dpc")
    core = lax.axis_index("core")
    view = part.reshape(blocks, n_chip, 2, rows // (2 * n_chip), cols)
    mine = jnp.where(core == 0, view[:, :, 0], view[:, :, 1])
    other = jnp.where(core == 0, view[:, :, 1], view[:, :, 0])
    got = lax.ppermute(other, "core", perm=[(0, 1), (1, 0)])
    summed = (mine.astype(jnp.float32) + got.astype(jnp.float32)).astype(jnp.bfloat16)
    summed = summed.reshape(blocks, rows // 2, cols)
    return lax.psum_scatter(summed, "dpc", scatter_dimension=1, tiled=True).astype(jnp.float32)


def local(features, cotangent, block_perm, w_gate, w_up, w_down):
    tok_count = features.shape[1]
    blocks_here = w_gate.shape[0]
    inner = w_gate.shape[1]
    hidden_width = w_gate.shape[2]
    n_mp = lax.axis_size("mp")
    n_chip = lax.axis_size("dpc")
    n_dp = n_chip * lax.axis_size("core")
    block_total = blocks_here * n_mp
    piece = inner // block_total
    s_here = features.shape[0] // (block_total * piece)
    grad_scale = (tok_count * n_dp) ** (-0.5)

    both = jnp.stack([features, cotangent]).reshape(2, s_here, block_total, piece, tok_count)
    both = lax.all_to_all(both, "mp", split_axis=2, concat_axis=1, tiled=True)
    feat_blocks = both[0]
    cot_blocks = both[1]

    onehot = perm_matrix(block_perm)
    feat_rows = feat_blocks.transpose(1, 0, 2, 3).reshape(blocks_here, inner, tok_count)
    feat_p = jnp.einsum(
        "bij,bjt->bit", onehot, feat_rows, preferred_element_type=jnp.float32
    ).astype(jnp.bfloat16)

    gate = (
        jnp.einsum("bit,bih->bth", feat_p, w_gate, preferred_element_type=jnp.float32)
        * input_scale
    )
    up = (
        jnp.einsum("bit,bih->bth", feat_p, w_up, preferred_element_type=jnp.float32)
        * input_scale
    )
    sig = jax.nn.sigmoid(gate)
    act = gate * sig
    hidden = (act * up).astype(jnp.bfloat16)
    down_view = w_down.reshape(blocks_here, hidden_width, block_total, piece)

    down_part = (
        jnp.einsum("bth,sbkt->bhsk", hidden, cot_blocks, preferred_element_type=jnp.float32)
        * (output_scale * grad_scale)
    ).astype(jnp.bfloat16)
    down_grad = reduce_rows(down_part.reshape(blocks_here, hidden_width, inner))

    mixed = (
        jnp.einsum("bth,bhsk->sbkt", hidden, down_view, preferred_element_type=jnp.float32)
        * output_scale
    ).astype(jnp.bfloat16)

    d_hidden = (
        jnp.einsum("sbkt,bhsk->bth", cot_blocks, down_view, preferred_element_type=jnp.float32)
        * output_scale
    )
    d_gate = (d_hidden * up * (sig * (1.0 + gate * (1.0 - sig)))).astype(jnp.bfloat16)
    d_up = (d_hidden * act).astype(jnp.bfloat16)

    gate_part = (
        jnp.einsum("bit,bth->bih", feat_p, d_gate, preferred_element_type=jnp.float32)
        * (input_scale * grad_scale)
    ).astype(jnp.bfloat16)
    up_part = (
        jnp.einsum("bit,bth->bih", feat_p, d_up, preferred_element_type=jnp.float32)
        * (input_scale * grad_scale)
    ).astype(jnp.bfloat16)
    gate_grad = reduce_rows(gate_part)
    up_grad = reduce_rows(up_part)

    d_mixed_p = (
        (
            jnp.einsum("bth,bih->bit", d_gate, w_gate, preferred_element_type=jnp.float32)
            + jnp.einsum("bth,bih->bit", d_up, w_up, preferred_element_type=jnp.float32)
        )
        * input_scale
    ).astype(jnp.bfloat16)
    d_mixed = jnp.einsum(
        "bij,bit->bjt", onehot, d_mixed_p, preferred_element_type=jnp.float32
    ).astype(jnp.bfloat16)
    d_mixed = d_mixed.reshape(blocks_here, block_total, piece, tok_count).transpose(1, 0, 2, 3)

    back = jnp.stack([mixed, d_mixed])
    back = lax.all_to_all(back, "mp", split_axis=1, concat_axis=2, tiled=True)
    outputs = back[0].reshape(features.shape)
    d_features = back[1].reshape(features.shape)
    return (outputs, d_features, gate_grad, up_grad, down_grad)


def solution(mesh):
    dp_size = mesh.shape["dp"]
    devices = mesh.devices.reshape(dp_size // 2, 2, mesh.shape["mp"])
    mesh = Mesh(devices, ("dpc", "core", "mp"))
    dp = ("dpc", "core")
    placed = (
        P("mp", dp),
        P("mp", dp),
        P("mp", None),
        P("mp", None, None),
        P("mp", None, None),
        P("mp", None, None),
    )
    return jax.shard_map(
        local,
        mesh=mesh,
        in_specs=placed,
        out_specs=(
            P("mp", dp),
            P("mp", dp),
            P("mp", dp, None),
            P("mp", dp, None),
            P("mp", dp, None),
        ),
        check_vma=False,
    )
```

```python
import jax
import jax.numpy as jnp
from jax import lax
from jax.sharding import Mesh
from jax.sharding import PartitionSpec as P

input_scale = 2.0
output_scale = 0.5


def perm_matrix(block_perm):
    count = block_perm.shape[1]
    targets = lax.broadcasted_iota(jnp.int32, (1, 1, count), 2)
    return (block_perm[:, :, None] == targets).astype(jnp.bfloat16)


def tree_reduce(part):
    lead, rows, cols = part.shape
    n_dy = lax.axis_size("dy")
    tail = rows // (n_dy * 4)
    acc = part.reshape(lead, n_dy // 2, 2, 2, 2, tail, cols)
    dy = lax.axis_index("dy")
    steps = (
        ("core", 4, [(0, 1), (1, 0)], lax.axis_index("core")),
        ("dy", 2, [(i, i ^ 1) for i in range(n_dy)], dy % 2),
        ("dz", 3, [(0, 1), (1, 0)], lax.axis_index("dz")),
        ("dy", 1, [(i, i ^ 2) for i in range(n_dy)], dy // 2),
    )
    total = None
    for name, dim, pairs, bit in steps:
        mine = lax.dynamic_index_in_dim(acc, bit, dim, keepdims=True)
        other = lax.dynamic_index_in_dim(acc, 1 - bit, dim, keepdims=True)
        got = lax.ppermute(other, name, perm=pairs)
        total = mine.astype(jnp.float32) + got.astype(jnp.float32)
        acc = total.astype(jnp.bfloat16)
    return total.reshape(lead, tail, cols)


def local(features, cotangent, block_perm, w_gate, w_up, w_down):
    tok_count = features.shape[1]
    blocks_here = w_gate.shape[0]
    inner = w_gate.shape[1]
    hidden_width = w_gate.shape[2]
    n_mp = lax.axis_size("mp")
    n_dp = lax.axis_size("dy") * lax.axis_size("dz") * lax.axis_size("core")
    block_total = blocks_here * n_mp
    piece = inner // block_total
    s_here = features.shape[0] // (block_total * piece)
    grad_scale = (tok_count * n_dp) ** (-0.5)

    both = jnp.stack([features, cotangent]).reshape(2, s_here, block_total, piece, tok_count)
    both = lax.all_to_all(both, "mp", split_axis=2, concat_axis=1, tiled=True)
    feat_blocks = both[0]
    cot_blocks = both[1]

    onehot = perm_matrix(block_perm)
    feat_rows = feat_blocks.transpose(1, 0, 2, 3).reshape(blocks_here, inner, tok_count)
    feat_p = jnp.einsum(
        "bij,bjt->bit", onehot, feat_rows, preferred_element_type=jnp.float32
    ).astype(jnp.bfloat16)

    gate = (
        jnp.einsum("bit,bih->bth", feat_p, w_gate, preferred_element_type=jnp.float32)
        * input_scale
    )
    up = (
        jnp.einsum("bit,bih->bth", feat_p, w_up, preferred_element_type=jnp.float32)
        * input_scale
    )
    sig = jax.nn.sigmoid(gate)
    act = gate * sig
    hidden = (act * up).astype(jnp.bfloat16)
    down_view = w_down.reshape(blocks_here, hidden_width, block_total, piece)

    down_part = (
        jnp.einsum("bth,sbkt->bhsk", hidden, cot_blocks, preferred_element_type=jnp.float32)
        * (output_scale * grad_scale)
    ).astype(jnp.bfloat16)
    down_grad = tree_reduce(down_part.reshape(blocks_here, hidden_width, inner))

    mixed = (
        jnp.einsum("bth,bhsk->sbkt", hidden, down_view, preferred_element_type=jnp.float32)
        * output_scale
    ).astype(jnp.bfloat16)

    d_hidden = (
        jnp.einsum("sbkt,bhsk->bth", cot_blocks, down_view, preferred_element_type=jnp.float32)
        * output_scale
    )
    d_gate = (d_hidden * up * (sig * (1.0 + gate * (1.0 - sig)))).astype(jnp.bfloat16)
    d_up = (d_hidden * act).astype(jnp.bfloat16)

    gate_part = (
        jnp.einsum("bit,bth->bih", feat_p, d_gate, preferred_element_type=jnp.float32)
        * (input_scale * grad_scale)
    ).astype(jnp.bfloat16)
    up_part = (
        jnp.einsum("bit,bth->bih", feat_p, d_up, preferred_element_type=jnp.float32)
        * (input_scale * grad_scale)
    ).astype(jnp.bfloat16)
    gate_up = tree_reduce(
        jnp.concatenate([gate_part, up_part]).reshape(2 * blocks_here, inner, hidden_width)
    )
    gate_grad = gate_up[:blocks_here]
    up_grad = gate_up[blocks_here:]

    d_mixed_p = (
        (
            jnp.einsum("bth,bih->bit", d_gate, w_gate, preferred_element_type=jnp.float32)
            + jnp.einsum("bth,bih->bit", d_up, w_up, preferred_element_type=jnp.float32)
        )
        * input_scale
    ).astype(jnp.bfloat16)
    d_mixed = jnp.einsum(
        "bij,bit->bjt", onehot, d_mixed_p, preferred_element_type=jnp.float32
    ).astype(jnp.bfloat16)
    d_mixed = d_mixed.reshape(blocks_here, block_total, piece, tok_count).transpose(1, 0, 2, 3)

    back = jnp.stack([mixed, d_mixed])
    back = lax.all_to_all(back, "mp", split_axis=1, concat_axis=2, tiled=True)
    outputs = back[0].reshape(features.shape)
    d_features = back[1].reshape(features.shape)
    return (outputs, d_features, gate_grad, up_grad, down_grad)


def solution(mesh):
    dp_size = mesh.shape["dp"]
    devices = mesh.devices.reshape(dp_size // 4, 2, 2, mesh.shape["mp"])
    mesh = Mesh(devices, ("dy", "dz", "core", "mp"))
    dp = ("dy", "dz", "core")
    placed = (
        P("mp", dp),
        P("mp", dp),
        P("mp", None),
        P("mp", None, None),
        P("mp", None, None),
        P("mp", None, None),
    )
    return jax.shard_map(
        local,
        mesh=mesh,
        in_specs=placed,
        out_specs=(
            P("mp", dp),
            P("mp", dp),
            P("mp", dp, None),
            P("mp", dp, None),
            P("mp", dp, None),
        ),
        check_vma=False,
    )
```

```python
import jax
import jax.numpy as jnp
from jax import lax
from jax.sharding import Mesh
from jax.sharding import PartitionSpec as P

input_scale = 2.0
output_scale = 0.5


def perm_matrix(block_perm):
    count = block_perm.shape[1]
    targets = lax.broadcasted_iota(jnp.int32, (1, 1, count), 2)
    return (block_perm[:, :, None] == targets).astype(jnp.bfloat16)


def own_bits():
    dy = lax.axis_index("dy")
    return (lax.axis_index("core"), dy % 2, lax.axis_index("dz"), dy // 2)


def relabel(x, axis):
    core, dy0, dz, dy1 = own_bits()
    for offset, bit in ((0, dy1), (1, dy0), (2, dz), (3, core)):
        x = jnp.where(bit == 1, jnp.flip(x, axis + offset), x)
    order = [axis + 3, axis + 1, axis + 2, axis] + [
        d for d in range(x.ndim) if d not in range(axis, axis + 4)
    ]
    return x.transpose(order)


def tree_reduce(acc):
    n_dy = lax.axis_size("dy")
    steps = (
        ("core", [(0, 1), (1, 0)]),
        ("dy", [(i, i ^ 1) for i in range(n_dy)]),
        ("dz", [(0, 1), (1, 0)]),
        ("dy", [(i, i ^ 2) for i in range(n_dy)]),
    )
    total = None
    for name, pairs in steps:
        got = lax.ppermute(acc[1], name, perm=pairs)
        total = acc[0].astype(jnp.float32) + got.astype(jnp.float32)
        acc = total.astype(jnp.bfloat16)
    return total


def local(features, cotangent, block_perm, w_gate, w_up, w_down):
    tok_count = features.shape[1]
    blocks_here = w_gate.shape[0]
    inner = w_gate.shape[1]
    hidden_width = w_gate.shape[2]
    n_mp = lax.axis_size("mp")
    n_dp = lax.axis_size("dy") * lax.axis_size("dz") * lax.axis_size("core")
    block_total = blocks_here * n_mp
    piece = inner // block_total
    s_here = features.shape[0] // (block_total * piece)
    grad_scale = (tok_count * n_dp) ** (-0.5)

    both = jnp.stack([features, cotangent]).reshape(2, s_here, block_total, piece, tok_count)
    both = lax.all_to_all(both, "mp", split_axis=2, concat_axis=1, tiled=True)
    feat_blocks = both[0]
    cot_blocks = both[1]

    onehot = perm_matrix(block_perm)
    feat_rows = feat_blocks.transpose(1, 0, 2, 3).reshape(blocks_here, inner, tok_count)
    feat_p = jnp.einsum(
        "bij,bjt->bit", onehot, feat_rows, preferred_element_type=jnp.float32
    ).astype(jnp.bfloat16)

    gate = (
        jnp.einsum("bit,bih->bth", feat_p, w_gate, preferred_element_type=jnp.float32)
        * input_scale
    )
    up = (
        jnp.einsum("bit,bih->bth", feat_p, w_up, preferred_element_type=jnp.float32)
        * input_scale
    )
    sig = jax.nn.sigmoid(gate)
    act = gate * sig
    hidden = (act * up).astype(jnp.bfloat16)
    down_view = w_down.reshape(blocks_here, hidden_width, block_total, piece)

    n_dy = lax.axis_size("dy")
    cot_rows = cot_blocks.transpose(1, 0, 2, 3).reshape(blocks_here, inner, tok_count)
    hid_l = relabel(
        hidden.reshape(blocks_here, tok_count, n_dy // 2, 2, 2, 2, hidden_width // (4 * n_dy)), 2
    )
    down_part = (
        jnp.einsum("cyzwbtr,bjt->cyzwbrj", hid_l, cot_rows, preferred_element_type=jnp.float32)
        * (output_scale * grad_scale)
    ).astype(jnp.bfloat16)
    down_grad = tree_reduce(down_part.reshape((2, 2, 2, 2) + down_part.shape[4:])).reshape(
        blocks_here, -1, inner
    )

    mixed = (
        jnp.einsum("bth,bhsk->sbkt", hidden, down_view, preferred_element_type=jnp.float32)
        * output_scale
    ).astype(jnp.bfloat16)

    d_hidden = (
        jnp.einsum("sbkt,bhsk->bth", cot_blocks, down_view, preferred_element_type=jnp.float32)
        * output_scale
    )
    d_gate = (d_hidden * up * (sig * (1.0 + gate * (1.0 - sig)))).astype(jnp.bfloat16)
    d_up = (d_hidden * act).astype(jnp.bfloat16)

    feat_l = relabel(
        feat_p.reshape(blocks_here, n_dy // 2, 2, 2, 2, inner // (4 * n_dy), tok_count), 1
    )
    d_both = jnp.stack([d_gate, d_up])
    gate_up_part = (
        jnp.einsum("cyzwbrt,gbth->cyzwgbrh", feat_l, d_both, preferred_element_type=jnp.float32)
        * (input_scale * grad_scale)
    ).astype(jnp.bfloat16)
    gate_up = tree_reduce(gate_up_part.reshape((2, 2, 2, 2) + gate_up_part.shape[4:]))
    gate_grad = gate_up[0]
    up_grad = gate_up[1]

    d_mixed_p = (
        (
            jnp.einsum("bth,bih->bit", d_gate, w_gate, preferred_element_type=jnp.float32)
            + jnp.einsum("bth,bih->bit", d_up, w_up, preferred_element_type=jnp.float32)
        )
        * input_scale
    ).astype(jnp.bfloat16)
    d_mixed = jnp.einsum(
        "bij,bit->bjt", onehot, d_mixed_p, preferred_element_type=jnp.float32
    ).astype(jnp.bfloat16)
    d_mixed = d_mixed.reshape(blocks_here, block_total, piece, tok_count).transpose(1, 0, 2, 3)

    back = jnp.stack([mixed, d_mixed])
    back = lax.all_to_all(back, "mp", split_axis=1, concat_axis=2, tiled=True)
    outputs = back[0].reshape(features.shape)
    d_features = back[1].reshape(features.shape)
    return (outputs, d_features, gate_grad, up_grad, down_grad)


def solution(mesh):
    dp_size = mesh.shape["dp"]
    devices = mesh.devices.reshape(dp_size // 4, 2, 2, mesh.shape["mp"])
    mesh = Mesh(devices, ("dy", "dz", "core", "mp"))
    dp = ("dy", "dz", "core")
    placed = (
        P("mp", dp),
        P("mp", dp),
        P("mp", None),
        P("mp", None, None),
        P("mp", None, None),
        P("mp", None, None),
    )
    return jax.shard_map(
        local,
        mesh=mesh,
        in_specs=placed,
        out_specs=(
            P("mp", dp),
            P("mp", dp),
            P("mp", dp, None),
            P("mp", dp, None),
            P("mp", dp, None),
        ),
        check_vma=False,
    )
```

```python
import jax
import jax.numpy as jnp
from jax import lax
from jax.sharding import Mesh
from jax.sharding import PartitionSpec as P

input_scale = 2.0
output_scale = 0.5


def perm_matrix(block_perm):
    count = block_perm.shape[1]
    targets = lax.broadcasted_iota(jnp.int32, (1, 1, count), 2)
    return (block_perm[:, :, None] == targets).astype(jnp.bfloat16)


def own_bits():
    dy = lax.axis_index("dy")
    return (lax.axis_index("core"), dy % 2, lax.axis_index("dz"), dy // 2)


def relabel(x, axis):
    core, dy0, dz, dy1 = own_bits()
    for offset, bit in ((0, dy1), (1, dy0), (2, dz), (3, core)):
        x = jnp.where(bit == 1, jnp.flip(x, axis + offset), x)
    order = [axis + 3, axis + 1, axis + 2, axis] + [
        d for d in range(x.ndim) if d not in range(axis, axis + 4)
    ]
    return x.transpose(order)


def tree_reduce(acc, order):
    n_dy = lax.axis_size("dy")
    swaps = {
        "core": ("core", [(0, 1), (1, 0)]),
        "dy0": ("dy", [(i, i ^ 1) for i in range(n_dy)]),
        "dz": ("dz", [(0, 1), (1, 0)]),
        "dy1": ("dy", [(i, i ^ 2) for i in range(n_dy)]),
    }
    dims = ["core", "dy0", "dz", "dy1"]
    total = None
    for bit in order:
        axis = dims.index(bit)
        dims.pop(axis)
        name, pairs = swaps[bit]
        got = lax.ppermute(lax.index_in_dim(acc, 1, axis, keepdims=False), name, perm=pairs)
        total = lax.index_in_dim(acc, 0, axis, keepdims=False).astype(jnp.float32) + got.astype(
            jnp.float32
        )
        acc = total.astype(jnp.bfloat16)
    return total


ORDER_A = ("core", "dy0", "dz", "dy1")
ORDER_B = ("core", "dz", "dy0", "dy1")


def local(features, cotangent, block_perm, w_gate, w_up, w_down):
    tok_count = features.shape[1]
    blocks_here = w_gate.shape[0]
    inner = w_gate.shape[1]
    hidden_width = w_gate.shape[2]
    n_mp = lax.axis_size("mp")
    n_dp = lax.axis_size("dy") * lax.axis_size("dz") * lax.axis_size("core")
    block_total = blocks_here * n_mp
    piece = inner // block_total
    s_here = features.shape[0] // (block_total * piece)
    grad_scale = (tok_count * n_dp) ** (-0.5)

    both = jnp.stack([features, cotangent]).reshape(2, s_here, block_total, piece, tok_count)
    both = lax.all_to_all(both, "mp", split_axis=2, concat_axis=1, tiled=True)
    feat_blocks = both[0]
    cot_blocks = both[1]

    onehot = perm_matrix(block_perm)
    feat_rows = feat_blocks.transpose(1, 0, 2, 3).reshape(blocks_here, inner, tok_count)
    feat_p = jnp.einsum(
        "bij,bjt->bit", onehot, feat_rows, preferred_element_type=jnp.float32
    ).astype(jnp.bfloat16)

    gate = (
        jnp.einsum("bit,bih->bth", feat_p, w_gate, preferred_element_type=jnp.float32)
        * input_scale
    )
    up = (
        jnp.einsum("bit,bih->bth", feat_p, w_up, preferred_element_type=jnp.float32)
        * input_scale
    )
    sig = jax.nn.sigmoid(gate)
    act = gate * sig
    hidden = (act * up).astype(jnp.bfloat16)
    down_view = w_down.reshape(blocks_here, hidden_width, block_total, piece)

    n_dy = lax.axis_size("dy")
    cot_rows = cot_blocks.transpose(1, 0, 2, 3).reshape(blocks_here, inner, tok_count)
    hid_l = relabel(
        hidden.reshape(blocks_here, tok_count, n_dy // 2, 2, 2, 2, hidden_width // (4 * n_dy)), 2
    )
    down_part = (
        jnp.einsum("cyzwbtr,bjt->bcyzwrj", hid_l, cot_rows, preferred_element_type=jnp.float32)
        * (output_scale * grad_scale)
    ).astype(jnp.bfloat16)
    down_grad = jnp.stack(
        [tree_reduce(down_part[b], (ORDER_A, ORDER_B)[b % 2]) for b in range(blocks_here)]
    )

    mixed = (
        jnp.einsum("bth,bhsk->sbkt", hidden, down_view, preferred_element_type=jnp.float32)
        * output_scale
    ).astype(jnp.bfloat16)

    d_hidden = (
        jnp.einsum("sbkt,bhsk->bth", cot_blocks, down_view, preferred_element_type=jnp.float32)
        * output_scale
    )
    d_gate = (d_hidden * up * (sig * (1.0 + gate * (1.0 - sig)))).astype(jnp.bfloat16)
    d_up = (d_hidden * act).astype(jnp.bfloat16)

    feat_l = relabel(
        feat_p.reshape(blocks_here, n_dy // 2, 2, 2, 2, inner // (4 * n_dy), tok_count), 1
    )
    d_both = jnp.stack([d_gate, d_up])
    gate_up_part = (
        jnp.einsum("cyzwbrt,gbth->gcyzwbrh", feat_l, d_both, preferred_element_type=jnp.float32)
        * (input_scale * grad_scale)
    ).astype(jnp.bfloat16)
    gate_grad = tree_reduce(gate_up_part[0], ORDER_A)
    up_grad = tree_reduce(gate_up_part[1], ORDER_B)

    d_mixed_p = (
        (
            jnp.einsum("bth,bih->bit", d_gate, w_gate, preferred_element_type=jnp.float32)
            + jnp.einsum("bth,bih->bit", d_up, w_up, preferred_element_type=jnp.float32)
        )
        * input_scale
    ).astype(jnp.bfloat16)
    d_mixed = jnp.einsum(
        "bij,bit->bjt", onehot, d_mixed_p, preferred_element_type=jnp.float32
    ).astype(jnp.bfloat16)
    d_mixed = d_mixed.reshape(blocks_here, block_total, piece, tok_count).transpose(1, 0, 2, 3)

    back = jnp.stack([mixed, d_mixed])
    back = lax.all_to_all(back, "mp", split_axis=1, concat_axis=2, tiled=True)
    outputs = back[0].reshape(features.shape)
    d_features = back[1].reshape(features.shape)
    return (outputs, d_features, gate_grad, up_grad, down_grad)


def solution(mesh):
    dp_size = mesh.shape["dp"]
    devices = mesh.devices.reshape(dp_size // 4, 2, 2, mesh.shape["mp"])
    mesh = Mesh(devices, ("dy", "dz", "core", "mp"))
    dp = ("dy", "dz", "core")
    placed = (
        P("mp", dp),
        P("mp", dp),
        P("mp", None),
        P("mp", None, None),
        P("mp", None, None),
        P("mp", None, None),
    )
    return jax.shard_map(
        local,
        mesh=mesh,
        in_specs=placed,
        out_specs=(
            P("mp", dp),
            P("mp", dp),
            P("mp", dp, None),
            P("mp", dp, None),
            P("mp", dp, None),
        ),
        check_vma=False,
    )
```

```python
import jax
import jax.numpy as jnp
from jax import lax
from jax.sharding import Mesh
from jax.sharding import PartitionSpec as P

input_scale = 2.0
output_scale = 0.5


def perm_matrix(block_perm):
    count = block_perm.shape[1]
    targets = lax.broadcasted_iota(jnp.int32, (1, 1, count), 2)
    return (block_perm[:, :, None] == targets).astype(jnp.bfloat16)


def own_bits():
    dy = lax.axis_index("dy")
    return (lax.axis_index("core"), dy % 2, lax.axis_index("dz"), dy // 2)


def relabel(x, axis):
    core, dy0, dz, dy1 = own_bits()
    for offset, bit in ((0, dy1), (1, dy0), (2, dz), (3, core)):
        x = jnp.where(bit == 1, jnp.flip(x, axis + offset), x)
    return x


def tree_reduce(acc, order, first):
    n_dy = lax.axis_size("dy")
    swaps = {
        "core": ("core", [(0, 1), (1, 0)]),
        "dy0": ("dy", [(i, i ^ 1) for i in range(n_dy)]),
        "dz": ("dz", [(0, 1), (1, 0)]),
        "dy1": ("dy", [(i, i ^ 2) for i in range(n_dy)]),
    }
    dims = ["dy1", "dy0", "dz", "core"]
    total = None
    for bit in order:
        axis = first + dims.index(bit)
        dims.remove(bit)
        name, pairs = swaps[bit]
        got = lax.ppermute(lax.index_in_dim(acc, 1, axis, keepdims=False), name, perm=pairs)
        total = lax.index_in_dim(acc, 0, axis, keepdims=False).astype(jnp.float32) + got.astype(
            jnp.float32
        )
        acc = total.astype(jnp.bfloat16)
    return total


ORDER_A = ("core", "dy0", "dz", "dy1")
ORDER_B = ("core", "dz", "dy0", "dy1")


def local(features, cotangent, block_perm, w_gate, w_up, w_down):
    tok_count = features.shape[1]
    blocks_here = w_gate.shape[0]
    inner = w_gate.shape[1]
    hidden_width = w_gate.shape[2]
    n_mp = lax.axis_size("mp")
    n_dp = lax.axis_size("dy") * lax.axis_size("dz") * lax.axis_size("core")
    block_total = blocks_here * n_mp
    piece = inner // block_total
    s_here = features.shape[0] // (block_total * piece)
    grad_scale = (tok_count * n_dp) ** (-0.5)

    local_shape = (s_here, block_total, piece, tok_count)
    feat_blocks = lax.all_to_all(
        features.reshape(local_shape), "mp", split_axis=1, concat_axis=0, tiled=True
    )
    cot_blocks = lax.all_to_all(
        cotangent.reshape(local_shape), "mp", split_axis=1, concat_axis=0, tiled=True
    )

    onehot = perm_matrix(block_perm)
    feat_rows = feat_blocks.transpose(1, 0, 2, 3).reshape(blocks_here, inner, tok_count)
    feat_p = jnp.einsum(
        "bij,bjt->bit", onehot, feat_rows, preferred_element_type=jnp.float32
    ).astype(jnp.bfloat16)

    gate = (
        jnp.einsum("bit,bih->bth", feat_p, w_gate, preferred_element_type=jnp.float32)
        * input_scale
    )
    up = (
        jnp.einsum("bit,bih->bth", feat_p, w_up, preferred_element_type=jnp.float32)
        * input_scale
    )
    sig = jax.nn.sigmoid(gate)
    act = gate * sig
    hidden = (act * up).astype(jnp.bfloat16)
    down_view = w_down.reshape(blocks_here, hidden_width, block_total, piece)

    n_dy = lax.axis_size("dy")
    cot_rows = cot_blocks.transpose(1, 0, 2, 3).reshape(blocks_here, inner, tok_count)
    hid_l = relabel(
        hidden.transpose(0, 2, 1).reshape(
            blocks_here, n_dy // 2, 2, 2, 2, hidden_width // (4 * n_dy), tok_count
        ),
        1,
    )
    down_part = (
        jnp.einsum("bwyzcrt,bjt->bwyzcrj", hid_l, cot_rows, preferred_element_type=jnp.float32)
        * (output_scale * grad_scale)
    ).astype(jnp.bfloat16)
    down_grad = jnp.stack(
        [tree_reduce(down_part[b], (ORDER_A, ORDER_B)[b % 2], 0) for b in range(blocks_here)]
    )

    mixed = (
        jnp.einsum("bth,bhsk->sbkt", hidden, down_view, preferred_element_type=jnp.float32)
        * output_scale
    ).astype(jnp.bfloat16)

    d_hidden = (
        jnp.einsum("sbkt,bhsk->bth", cot_blocks, down_view, preferred_element_type=jnp.float32)
        * output_scale
    )
    d_gate = (d_hidden * up * (sig * (1.0 + gate * (1.0 - sig)))).astype(jnp.bfloat16)
    d_up = (d_hidden * act).astype(jnp.bfloat16)

    feat_l = relabel(
        feat_p.reshape(blocks_here, n_dy // 2, 2, 2, 2, inner // (4 * n_dy), tok_count), 1
    )
    d_both = jnp.stack([d_gate, d_up])
    gate_up_part = (
        jnp.einsum("bwyzcrt,gbth->gbwyzcrh", feat_l, d_both, preferred_element_type=jnp.float32)
        * (input_scale * grad_scale)
    ).astype(jnp.bfloat16)
    gate_grad = tree_reduce(gate_up_part[0], ORDER_A, 1)
    up_grad = tree_reduce(gate_up_part[1], ORDER_B, 1)

    d_mixed_p = (
        (
            jnp.einsum("bth,bih->bit", d_gate, w_gate, preferred_element_type=jnp.float32)
            + jnp.einsum("bth,bih->bit", d_up, w_up, preferred_element_type=jnp.float32)
        )
        * input_scale
    ).astype(jnp.bfloat16)
    d_mixed = jnp.einsum(
        "bij,bit->bjt", onehot, d_mixed_p, preferred_element_type=jnp.float32
    ).astype(jnp.bfloat16)
    d_mixed = d_mixed.reshape(blocks_here, block_total, piece, tok_count).transpose(1, 0, 2, 3)

    back = jnp.stack([mixed, d_mixed])
    back = lax.all_to_all(back, "mp", split_axis=1, concat_axis=2, tiled=True)
    outputs = back[0].reshape(features.shape)
    d_features = back[1].reshape(features.shape)
    return (outputs, d_features, gate_grad, up_grad, down_grad)


def solution(mesh):
    dp_size = mesh.shape["dp"]
    devices = mesh.devices.reshape(dp_size // 4, 2, 2, mesh.shape["mp"])
    mesh = Mesh(devices, ("dy", "dz", "core", "mp"))
    dp = ("dy", "dz", "core")
    placed = (
        P("mp", dp),
        P("mp", dp),
        P("mp", None),
        P("mp", None, None),
        P("mp", None, None),
        P("mp", None, None),
    )
    return jax.shard_map(
        local,
        mesh=mesh,
        in_specs=placed,
        out_specs=(
            P("mp", dp),
            P("mp", dp),
            P("mp", dp, None),
            P("mp", dp, None),
            P("mp", dp, None),
        ),
        check_vma=False,
    )
```

```python
import jax
import jax.numpy as jnp
from jax import lax
from jax.sharding import Mesh
from jax.sharding import PartitionSpec as P

input_scale = 2.0
output_scale = 0.5


def perm_matrix(block_perm):
    count = block_perm.shape[1]
    targets = lax.broadcasted_iota(jnp.int32, (1, 1, count), 2)
    return (block_perm[:, :, None] == targets).astype(jnp.bfloat16)


def own_bits():
    dy = lax.axis_index("dy")
    return (lax.axis_index("core"), dy % 2, lax.axis_index("dz"), dy // 2)


def relabel(x, axis):
    core, dy0, dz, dy1 = own_bits()
    for offset, bit in ((0, dy1), (1, dy0), (2, dz), (3, core)):
        x = jnp.where(bit == 1, jnp.flip(x, axis + offset), x)
    return x


def tree_reduce(acc, order, first):
    n_dy = lax.axis_size("dy")
    swaps = {
        "core": ("core", [(0, 1), (1, 0)]),
        "dy0": ("dy", [(i, i ^ 1) for i in range(n_dy)]),
        "dz": ("dz", [(0, 1), (1, 0)]),
        "dy1": ("dy", [(i, i ^ 2) for i in range(n_dy)]),
    }
    dims = ["dy1", "dy0", "dz", "core"]
    total = None
    for bit in order:
        axis = first + dims.index(bit)
        dims.remove(bit)
        name, pairs = swaps[bit]
        got = lax.ppermute(lax.index_in_dim(acc, 1, axis, keepdims=False), name, perm=pairs)
        total = lax.index_in_dim(acc, 0, axis, keepdims=False).astype(jnp.float32) + got.astype(
            jnp.float32
        )
        acc = total.astype(jnp.bfloat16)
    return total


ORDER_A = ("core", "dy0", "dz", "dy1")
ORDER_B = ("core", "dz", "dy0", "dy1")


def local(features, cotangent, block_perm, w_gate, w_up, w_down):
    tok_count = features.shape[1]
    blocks_here = w_gate.shape[0]
    inner = w_gate.shape[1]
    hidden_width = w_gate.shape[2]
    n_mp = lax.axis_size("mp")
    n_dp = lax.axis_size("dy") * lax.axis_size("dz") * lax.axis_size("core")
    block_total = blocks_here * n_mp
    piece = inner // block_total
    s_here = features.shape[0] // (block_total * piece)
    grad_scale = (tok_count * n_dp) ** (-0.5)

    both = jnp.stack([features, cotangent]).reshape(2, s_here, block_total, piece, tok_count)
    both = lax.all_to_all(both, "mp", split_axis=2, concat_axis=1, tiled=True)
    feat_blocks = both[0]
    cot_blocks = both[1]

    onehot = perm_matrix(block_perm)
    feat_rows = feat_blocks.transpose(1, 0, 2, 3).reshape(blocks_here, inner, tok_count)
    feat_p = jnp.einsum(
        "bij,bjt->bit", onehot, feat_rows, preferred_element_type=jnp.float32
    ).astype(jnp.bfloat16)

    gate = (
        jnp.einsum("bit,bih->bth", feat_p, w_gate, preferred_element_type=jnp.float32)
        * input_scale
    )
    up = (
        jnp.einsum("bit,bih->bth", feat_p, w_up, preferred_element_type=jnp.float32)
        * input_scale
    )
    sig = jax.nn.sigmoid(gate)
    act = gate * sig
    hidden = (act * up).astype(jnp.bfloat16)
    down_view = w_down.reshape(blocks_here, hidden_width, block_total, piece)

    n_dy = lax.axis_size("dy")
    cot_rows = cot_blocks.transpose(1, 0, 2, 3).reshape(blocks_here, inner, tok_count)
    hid_l = relabel(
        hidden.transpose(0, 2, 1).reshape(
            blocks_here, n_dy // 2, 2, 2, 2, hidden_width // (4 * n_dy), tok_count
        ),
        1,
    )
    down_part = (
        jnp.einsum("bwyzcrt,bjt->bwyzcrj", hid_l, cot_rows, preferred_element_type=jnp.float32)
        * (output_scale * grad_scale)
    ).astype(jnp.bfloat16)
    down_grad = jnp.stack(
        [tree_reduce(down_part[b], (ORDER_A, ORDER_B)[b % 2], 0) for b in range(blocks_here)]
    )

    mixed = (
        jnp.einsum("bth,bhsk->sbkt", hidden, down_view, preferred_element_type=jnp.float32)
        * output_scale
    ).astype(jnp.bfloat16)

    d_hidden = (
        jnp.einsum("sbkt,bhsk->bth", cot_blocks, down_view, preferred_element_type=jnp.float32)
        * output_scale
    )
    d_gate = (d_hidden * up * (sig * (1.0 + gate * (1.0 - sig)))).astype(jnp.bfloat16)
    d_up = (d_hidden * act).astype(jnp.bfloat16)

    feat_l = relabel(
        feat_p.reshape(blocks_here, n_dy // 2, 2, 2, 2, inner // (4 * n_dy), tok_count), 1
    )
    d_both = jnp.stack([d_gate, d_up])
    gate_up_part = (
        jnp.einsum("bwyzcrt,gbth->gbwyzcrh", feat_l, d_both, preferred_element_type=jnp.float32)
        * (input_scale * grad_scale)
    ).astype(jnp.bfloat16)
    gate_up_part, d_gate, d_up = lax.optimization_barrier((gate_up_part, d_gate, d_up))
    gate_grad = tree_reduce(gate_up_part[0], ORDER_A, 1)
    up_grad = tree_reduce(gate_up_part[1], ORDER_B, 1)

    d_mixed_p = (
        (
            jnp.einsum("bth,bih->bit", d_gate, w_gate, preferred_element_type=jnp.float32)
            + jnp.einsum("bth,bih->bit", d_up, w_up, preferred_element_type=jnp.float32)
        )
        * input_scale
    ).astype(jnp.bfloat16)
    d_mixed = jnp.einsum(
        "bij,bit->bjt", onehot, d_mixed_p, preferred_element_type=jnp.float32
    ).astype(jnp.bfloat16)
    d_mixed = d_mixed.reshape(blocks_here, block_total, piece, tok_count).transpose(1, 0, 2, 3)

    back = jnp.stack([mixed, d_mixed])
    back = lax.all_to_all(back, "mp", split_axis=1, concat_axis=2, tiled=True)
    outputs = back[0].reshape(features.shape)
    d_features = back[1].reshape(features.shape)
    return (outputs, d_features, gate_grad, up_grad, down_grad)


def solution(mesh):
    dp_size = mesh.shape["dp"]
    devices = mesh.devices.reshape(dp_size // 4, 2, 2, mesh.shape["mp"])
    mesh = Mesh(devices, ("dy", "dz", "core", "mp"))
    dp = ("dy", "dz", "core")
    placed = (
        P("mp", dp),
        P("mp", dp),
        P("mp", None),
        P("mp", None, None),
        P("mp", None, None),
        P("mp", None, None),
    )
    return jax.shard_map(
        local,
        mesh=mesh,
        in_specs=placed,
        out_specs=(
            P("mp", dp),
            P("mp", dp),
            P("mp", dp, None),
            P("mp", dp, None),
            P("mp", dp, None),
        ),
        check_vma=False,
    )
```

```python
import jax
import jax.numpy as jnp
from jax import lax
from jax.sharding import Mesh
from jax.sharding import PartitionSpec as P


input_scale = 2.0
output_scale = 0.5


def perm_matrix(block_perm):
    count = block_perm.shape[1]
    targets = lax.broadcasted_iota(jnp.int32, (1, 1, count), 2)
    return (block_perm[:, :, None] == targets).astype(jnp.bfloat16)


def own_bits():
    dy = lax.axis_index("dy")
    return (lax.axis_index("core"), dy % 2, lax.axis_index("dz"), dy // 2)


def relabel(x, axis):
    core, dy0, dz, dy1 = own_bits()
    for offset, bit in ((0, dy1), (1, dy0), (2, dz), (3, core)):
        x = jnp.where(bit == 1, jnp.flip(x, axis + offset), x)
    return x


def tree_reduce(acc, order, first):
    n_dy = lax.axis_size("dy")
    swaps = {
        "core": ("core", [(0, 1), (1, 0)]),
        "dy0": ("dy", [(i, i ^ 1) for i in range(n_dy)]),
        "dz": ("dz", [(0, 1), (1, 0)]),
        "dy1": ("dy", [(i, i ^ 2) for i in range(n_dy)]),
    }
    dims = ["dy1", "dy0", "dz", "core"]
    total = None
    for bit in order:
        axis = first + dims.index(bit)
        dims.remove(bit)
        name, pairs = swaps[bit]
        got = lax.ppermute(lax.index_in_dim(acc, 1, axis, keepdims=False), name, perm=pairs)
        total = lax.index_in_dim(acc, 0, axis, keepdims=False).astype(
            jnp.float32
        ) + got.astype(jnp.float32)
        acc = total.astype(jnp.bfloat16)
    return total


ORDER_A = ("core", "dy0", "dz", "dy1")
ORDER_B = ("core", "dz", "dy0", "dy1")


def local(features, cotangent, block_perm, w_gate, w_up, w_down):
    tok_count = features.shape[1]
    blocks_here = w_gate.shape[0]
    inner = w_gate.shape[1]
    hidden_width = w_gate.shape[2]
    n_mp = lax.axis_size("mp")
    n_dp = lax.axis_size("dy") * lax.axis_size("dz") * lax.axis_size("core")
    block_total = blocks_here * n_mp
    piece = inner // block_total
    s_here = features.shape[0] // (block_total * piece)
    grad_scale = (tok_count * n_dp) ** (-0.5)

    both = jnp.stack([features, cotangent]).reshape(2, s_here, block_total, piece, tok_count)
    both = lax.all_to_all(both, "mp", split_axis=2, concat_axis=1, tiled=True)
    feat_blocks = both[0]
    cot_blocks = both[1]

    onehot = perm_matrix(block_perm)
    feat_rows = feat_blocks.transpose(1, 0, 2, 3).reshape(blocks_here, inner, tok_count)
    feat_p = jnp.einsum(
        "bij,bjt->bit", onehot, feat_rows, preferred_element_type=jnp.float32
    ).astype(jnp.bfloat16)

    gate = (
        jnp.einsum("bit,bih->bth", feat_p, w_gate, preferred_element_type=jnp.float32)
        * input_scale
    )
    up = (
        jnp.einsum("bit,bih->bth", feat_p, w_up, preferred_element_type=jnp.float32)
        * input_scale
    )
    sig = jax.nn.sigmoid(gate)
    act = gate * sig
    hidden = (act * up).astype(jnp.bfloat16)
    down_view = w_down.reshape(blocks_here, hidden_width, block_total, piece)

    n_dy = lax.axis_size("dy")
    cot_rows = cot_blocks.transpose(1, 0, 2, 3).reshape(blocks_here, inner, tok_count)
    hid_l = relabel(
        hidden.transpose(0, 2, 1).reshape(
            blocks_here, n_dy // 2, 2, 2, 2, hidden_width // (4 * n_dy), tok_count
        ),
        1,
    )
    down_part = (
        jnp.einsum("bwyzcrt,bjt->bwyzcrj", hid_l, cot_rows, preferred_element_type=jnp.float32)
        * (output_scale * grad_scale)
    ).astype(jnp.bfloat16)
    down_grad = jnp.stack(
        [tree_reduce(down_part[b], (ORDER_A, ORDER_B)[b % 2], 0) for b in range(blocks_here)]
    )

    mixed = (
        jnp.einsum("bth,bhsk->sbkt", hidden, down_view, preferred_element_type=jnp.float32)
        * output_scale
    ).astype(jnp.bfloat16)
    outputs = lax.all_to_all(mixed, "mp", split_axis=0, concat_axis=1, tiled=True).reshape(
        features.shape
    )

    d_hidden = (
        jnp.einsum("sbkt,bhsk->bth", cot_blocks, down_view, preferred_element_type=jnp.float32)
        * output_scale
    )
    d_gate = (d_hidden * up * (sig * (1.0 + gate * (1.0 - sig)))).astype(jnp.bfloat16)
    d_up = (d_hidden * act).astype(jnp.bfloat16)

    feat_l = relabel(
        feat_p.reshape(blocks_here, n_dy // 2, 2, 2, 2, inner // (4 * n_dy), tok_count), 1
    )
    d_both = jnp.stack([d_gate, d_up])
    gate_up_part = (
        jnp.einsum(
            "bwyzcrt,gbth->gbwyzcrh", feat_l, d_both, preferred_element_type=jnp.float32
        )
        * (input_scale * grad_scale)
    ).astype(jnp.bfloat16)
    gate_up_part, d_gate, d_up = lax.optimization_barrier((gate_up_part, d_gate, d_up))
    gate_grad = tree_reduce(gate_up_part[0], ORDER_A, 1)
    up_grad = tree_reduce(gate_up_part[1], ORDER_B, 1)

    d_mixed_p = (
        (
            jnp.einsum("bth,bih->bit", d_gate, w_gate, preferred_element_type=jnp.float32)
            + jnp.einsum("bth,bih->bit", d_up, w_up, preferred_element_type=jnp.float32)
        )
        * input_scale
    ).astype(jnp.bfloat16)
    d_mixed = jnp.einsum(
        "bij,bit->bjt", onehot, d_mixed_p, preferred_element_type=jnp.float32
    ).astype(jnp.bfloat16)
    d_mixed = d_mixed.reshape(blocks_here, block_total, piece, tok_count).transpose(1, 0, 2, 3)

    d_features = lax.all_to_all(d_mixed, "mp", split_axis=0, concat_axis=1, tiled=True).reshape(
        features.shape
    )
    return (outputs, d_features, gate_grad, up_grad, down_grad)


def solution(mesh):
    dp_size = mesh.shape["dp"]
    devices = mesh.devices.reshape(dp_size // 4, 2, 2, mesh.shape["mp"])
    mesh = Mesh(devices, ("dy", "dz", "core", "mp"))
    dp = ("dy", "dz", "core")
    placed = (
        P("mp", dp),
        P("mp", dp),
        P("mp", None),
        P("mp", None, None),
        P("mp", None, None),
        P("mp", None, None),
    )

    return jax.shard_map(
        local,
        mesh=mesh,
        in_specs=placed,
        out_specs=(
            P("mp", dp),
            P("mp", dp),
            P("mp", dp, None),
            P("mp", dp, None),
            P("mp", dp, None),
        ),
        check_vma=False,
    )
```

```python
import jax
import jax.numpy as jnp
from jax import lax
from jax.sharding import Mesh
from jax.sharding import PartitionSpec as P


input_scale = 2.0
output_scale = 0.5


def perm_matrix(block_perm):
    count = block_perm.shape[1]
    targets = lax.broadcasted_iota(jnp.int32, (1, 1, count), 2)
    return (block_perm[:, :, None] == targets).astype(jnp.bfloat16)


def own_bits():
    dy = lax.axis_index("dy")
    return (lax.axis_index("core"), dy % 2, lax.axis_index("dz"), dy // 2)


def relabel(x, axis):
    core, dy0, dz, dy1 = own_bits()
    for offset, bit in ((0, dy1), (1, dy0), (2, dz), (3, core)):
        x = jnp.where(bit == 1, jnp.flip(x, axis + offset), x)
    return x


def tree_reduce(acc, order, first, dims=("dy1", "dy0", "dz", "core")):
    n_dy = lax.axis_size("dy")
    swaps = {
        "core": ("core", [(0, 1), (1, 0)]),
        "dy0": ("dy", [(i, i ^ 1) for i in range(n_dy)]),
        "dz": ("dz", [(0, 1), (1, 0)]),
        "dy1": ("dy", [(i, i ^ 2) for i in range(n_dy)]),
    }
    dims = list(dims)
    total = None
    for bit in order:
        axis = first + dims.index(bit)
        dims.remove(bit)
        name, pairs = swaps[bit]
        got = lax.ppermute(lax.index_in_dim(acc, 1, axis, keepdims=False), name, perm=pairs)
        total = lax.index_in_dim(acc, 0, axis, keepdims=False).astype(
            jnp.float32
        ) + got.astype(jnp.float32)
        acc = total.astype(jnp.bfloat16)
    return total


ORDER_A = ("core", "dy0", "dz", "dy1")
ORDER_B = ("core", "dz", "dy0", "dy1")


def local(features, cotangent, block_perm, w_gate, w_up, w_down):
    tok_count = features.shape[1]
    blocks_here = w_gate.shape[0]
    inner = w_gate.shape[1]
    hidden_width = w_gate.shape[2]
    n_mp = lax.axis_size("mp")
    n_dp = lax.axis_size("dy") * lax.axis_size("dz") * lax.axis_size("core")
    block_total = blocks_here * n_mp
    piece = inner // block_total
    s_here = features.shape[0] // (block_total * piece)
    grad_scale = (tok_count * n_dp) ** (-0.5)

    both = jnp.stack([features, cotangent]).reshape(2, s_here, block_total, piece, tok_count)
    both = lax.all_to_all(both, "mp", split_axis=2, concat_axis=1, tiled=True)
    feat_blocks = both[0]
    cot_blocks = both[1]

    onehot = perm_matrix(block_perm)
    feat_rows = feat_blocks.transpose(1, 0, 2, 3).reshape(blocks_here, inner, tok_count)
    feat_p = jnp.einsum(
        "bij,bjt->bit", onehot, feat_rows, preferred_element_type=jnp.float32
    ).astype(jnp.bfloat16)

    gate = (
        jnp.einsum("bit,bih->bth", feat_p, w_gate, preferred_element_type=jnp.float32)
        * input_scale
    )
    up = (
        jnp.einsum("bit,bih->bth", feat_p, w_up, preferred_element_type=jnp.float32)
        * input_scale
    )
    sig = jax.nn.sigmoid(gate)
    act = gate * sig
    hidden = (act * up).astype(jnp.bfloat16)
    down_view = w_down.reshape(blocks_here, hidden_width, block_total, piece)

    n_dy = lax.axis_size("dy")
    cot_rows = cot_blocks.transpose(1, 0, 2, 3).reshape(blocks_here, inner, tok_count)
    hid_l = relabel(
        hidden.transpose(0, 2, 1).reshape(
            blocks_here, n_dy // 2, 2, 2, 2, hidden_width // (4 * n_dy), tok_count
        ),
        1,
    )
    down_part = (
        jnp.einsum("bwyzcrt,bjt->bwyzcrj", hid_l, cot_rows, preferred_element_type=jnp.float32)
        * (output_scale * grad_scale)
    ).astype(jnp.bfloat16)
    down_grad = jnp.stack(
        [tree_reduce(down_part[b], (ORDER_A, ORDER_B)[b % 2], 0) for b in range(blocks_here)]
    )

    mixed = (
        jnp.einsum("bth,bhsk->sbkt", hidden, down_view, preferred_element_type=jnp.float32)
        * output_scale
    ).astype(jnp.bfloat16)
    outputs = lax.all_to_all(mixed, "mp", split_axis=0, concat_axis=1, tiled=True).reshape(
        features.shape
    )

    d_hidden = (
        jnp.einsum("sbkt,bhsk->bth", cot_blocks, down_view, preferred_element_type=jnp.float32)
        * output_scale
    )
    d_gate = (d_hidden * up * (sig * (1.0 + gate * (1.0 - sig)))).astype(jnp.bfloat16)
    d_up = (d_hidden * act).astype(jnp.bfloat16)

    feat_l = relabel(
        feat_p.reshape(blocks_here, n_dy // 2, 2, 2, 2, inner // (4 * n_dy), tok_count), 1
    )
    d_both = jnp.stack([d_gate, d_up])
    gate_up_part = (
        jnp.einsum(
            "bwyzcrt,gbth->gbwyzcrh", feat_l, d_both, preferred_element_type=jnp.float32
        )
        * (input_scale * grad_scale)
    ).astype(jnp.bfloat16)
    gate_core = tree_reduce(gate_up_part[0], ORDER_A[:1], 1).astype(jnp.bfloat16)
    up_core = tree_reduce(gate_up_part[1], ORDER_B[:1], 1).astype(jnp.bfloat16)
    gate_core, up_core, d_gate, d_up = lax.optimization_barrier((gate_core, up_core, d_gate, d_up))
    rest = ("dy1", "dy0", "dz")
    gate_grad = tree_reduce(gate_core, ORDER_A[1:], 1, rest)
    up_grad = tree_reduce(up_core, ORDER_B[1:], 1, rest)

    d_mixed_p = (
        (
            jnp.einsum("bth,bih->bit", d_gate, w_gate, preferred_element_type=jnp.float32)
            + jnp.einsum("bth,bih->bit", d_up, w_up, preferred_element_type=jnp.float32)
        )
        * input_scale
    ).astype(jnp.bfloat16)
    d_mixed = jnp.einsum(
        "bij,bit->bjt", onehot, d_mixed_p, preferred_element_type=jnp.float32
    ).astype(jnp.bfloat16)
    d_mixed = d_mixed.reshape(blocks_here, block_total, piece, tok_count).transpose(1, 0, 2, 3)

    d_features = lax.all_to_all(d_mixed, "mp", split_axis=0, concat_axis=1, tiled=True).reshape(
        features.shape
    )
    return (outputs, d_features, gate_grad, up_grad, down_grad)


def solution(mesh):
    dp_size = mesh.shape["dp"]
    devices = mesh.devices.reshape(dp_size // 4, 2, 2, mesh.shape["mp"])
    mesh = Mesh(devices, ("dy", "dz", "core", "mp"))
    dp = ("dy", "dz", "core")
    placed = (
        P("mp", dp),
        P("mp", dp),
        P("mp", None),
        P("mp", None, None),
        P("mp", None, None),
        P("mp", None, None),
    )

    return jax.shard_map(
        local,
        mesh=mesh,
        in_specs=placed,
        out_specs=(
            P("mp", dp),
            P("mp", dp),
            P("mp", dp, None),
            P("mp", dp, None),
            P("mp", dp, None),
        ),
        check_vma=False,
    )
```

```python
import jax
import jax.numpy as jnp
from jax import lax
from jax.sharding import Mesh
from jax.sharding import PartitionSpec as P


input_scale = 2.0
output_scale = 0.5


def perm_matrix(block_perm):
    count = block_perm.shape[1]
    targets = lax.broadcasted_iota(jnp.int32, (1, 1, count), 2)
    return (block_perm[:, :, None] == targets).astype(jnp.bfloat16)


def own_bits():
    dy = lax.axis_index("dy")
    return (lax.axis_index("core"), dy % 2, lax.axis_index("dz"), dy // 2)


def relabel(x, axis):
    core, dy0, dz, dy1 = own_bits()
    for offset, bit in ((0, dy1), (1, dy0), (2, dz), (3, core)):
        x = jnp.where(bit == 1, jnp.flip(x, axis + offset), x)
    return x


def tree_reduce(acc, order, first, dims=("dy1", "dy0", "dz", "core")):
    n_dy = lax.axis_size("dy")
    swaps = {
        "core": ("core", [(0, 1), (1, 0)]),
        "dy0": ("dy", [(i, i ^ 1) for i in range(n_dy)]),
        "dz": ("dz", [(0, 1), (1, 0)]),
        "dy1": ("dy", [(i, i ^ 2) for i in range(n_dy)]),
    }
    dims = list(dims)
    total = None
    for bit in order:
        axis = first + dims.index(bit)
        dims.remove(bit)
        name, pairs = swaps[bit]
        got = lax.ppermute(lax.index_in_dim(acc, 1, axis, keepdims=False), name, perm=pairs)
        total = lax.index_in_dim(acc, 0, axis, keepdims=False).astype(
            jnp.float32
        ) + got.astype(jnp.float32)
        acc = total.astype(jnp.bfloat16)
    return total


ORDER_A = ("core", "dy0", "dz", "dy1")
ORDER_B = ("core", "dz", "dy0", "dy1")


def local(features, cotangent, block_perm, w_gate, w_up, w_down):
    tok_count = features.shape[1]
    blocks_here = w_gate.shape[0]
    inner = w_gate.shape[1]
    hidden_width = w_gate.shape[2]
    n_mp = lax.axis_size("mp")
    n_dp = lax.axis_size("dy") * lax.axis_size("dz") * lax.axis_size("core")
    block_total = blocks_here * n_mp
    piece = inner // block_total
    s_here = features.shape[0] // (block_total * piece)
    grad_scale = (tok_count * n_dp) ** (-0.5)

    both = jnp.stack([features, cotangent]).reshape(2, s_here, block_total, piece, tok_count)
    both = lax.all_to_all(both, "mp", split_axis=2, concat_axis=1, tiled=True)
    feat_blocks = both[0]
    cot_blocks = both[1]

    onehot = perm_matrix(block_perm)
    feat_rows = feat_blocks.transpose(1, 0, 2, 3).reshape(blocks_here, inner, tok_count)
    feat_p = jnp.einsum(
        "bij,bjt->bit", onehot, feat_rows, preferred_element_type=jnp.float32
    ).astype(jnp.bfloat16)

    gate = (
        jnp.einsum("bit,bih->bth", feat_p, w_gate, preferred_element_type=jnp.float32)
        * input_scale
    )
    up = (
        jnp.einsum("bit,bih->bth", feat_p, w_up, preferred_element_type=jnp.float32)
        * input_scale
    )
    sig = jax.nn.sigmoid(gate)
    act = gate * sig
    hidden = (act * up).astype(jnp.bfloat16)
    down_view = w_down.reshape(blocks_here, hidden_width, block_total, piece)

    n_dy = lax.axis_size("dy")
    cot_rows = cot_blocks.transpose(1, 0, 2, 3).reshape(blocks_here, inner, tok_count)
    hid_l = relabel(
        hidden.transpose(0, 2, 1).reshape(
            blocks_here, n_dy // 2, 2, 2, 2, hidden_width // (4 * n_dy), tok_count
        ),
        1,
    )
    down_part = (
        jnp.einsum("bwyzcrt,bjt->bwyzcrj", hid_l, cot_rows, preferred_element_type=jnp.float32)
        * (output_scale * grad_scale)
    ).astype(jnp.bfloat16)
    down_orders = [(ORDER_A, ORDER_B)[b % 2] for b in range(blocks_here)]
    down_mid = [
        tree_reduce(down_part[b], down_orders[b][:2], 0).astype(jnp.bfloat16)
        for b in range(blocks_here)
    ]


    mixed = (
        jnp.einsum("bth,bhsk->sbkt", hidden, down_view, preferred_element_type=jnp.float32)
        * output_scale
    ).astype(jnp.bfloat16)
    outputs = lax.all_to_all(mixed, "mp", split_axis=0, concat_axis=1, tiled=True).reshape(
        features.shape
    )

    d_hidden = (
        jnp.einsum("sbkt,bhsk->bth", cot_blocks, down_view, preferred_element_type=jnp.float32)
        * output_scale
    )
    d_gate = (d_hidden * up * (sig * (1.0 + gate * (1.0 - sig)))).astype(jnp.bfloat16)
    d_up = (d_hidden * act).astype(jnp.bfloat16)

    feat_l = relabel(
        feat_p.reshape(blocks_here, n_dy // 2, 2, 2, 2, inner // (4 * n_dy), tok_count), 1
    )
    d_both = jnp.stack([d_gate, d_up])
    down_mid, feat_l, d_both = lax.optimization_barrier((down_mid, feat_l, d_both))
    down_grad = jnp.stack(
        [
            tree_reduce(
                down_mid[b],
                down_orders[b][2:],
                0,
                [d for d in ("dy1", "dy0", "dz") if d not in down_orders[b][:2]],
            )
            for b in range(blocks_here)
        ]
    )
    gate_up_part = (
        jnp.einsum(
            "bwyzcrt,gbth->gbwyzcrh", feat_l, d_both, preferred_element_type=jnp.float32
        )
        * (input_scale * grad_scale)
    ).astype(jnp.bfloat16)
    gate_core = tree_reduce(gate_up_part[0], ORDER_A[:1], 1).astype(jnp.bfloat16)
    up_core = tree_reduce(gate_up_part[1], ORDER_B[:1], 1).astype(jnp.bfloat16)
    gate_core, up_core, d_gate, d_up = lax.optimization_barrier((gate_core, up_core, d_gate, d_up))
    rest = ("dy1", "dy0", "dz")
    gate_grad = tree_reduce(gate_core, ORDER_A[1:], 1, rest)
    up_grad = tree_reduce(up_core, ORDER_B[1:], 1, rest)

    d_mixed_p = (
        (
            jnp.einsum("bth,bih->bit", d_gate, w_gate, preferred_element_type=jnp.float32)
            + jnp.einsum("bth,bih->bit", d_up, w_up, preferred_element_type=jnp.float32)
        )
        * input_scale
    ).astype(jnp.bfloat16)
    d_mixed = jnp.einsum(
        "bij,bit->bjt", onehot, d_mixed_p, preferred_element_type=jnp.float32
    ).astype(jnp.bfloat16)
    d_mixed = d_mixed.reshape(blocks_here, block_total, piece, tok_count).transpose(1, 0, 2, 3)

    d_features = lax.all_to_all(d_mixed, "mp", split_axis=0, concat_axis=1, tiled=True).reshape(
        features.shape
    )
    return (outputs, d_features, gate_grad, up_grad, down_grad)


def solution(mesh):
    dp_size = mesh.shape["dp"]
    devices = mesh.devices.reshape(dp_size // 4, 2, 2, mesh.shape["mp"])
    mesh = Mesh(devices, ("dy", "dz", "core", "mp"))
    dp = ("dy", "dz", "core")
    placed = (
        P("mp", dp),
        P("mp", dp),
        P("mp", None),
        P("mp", None, None),
        P("mp", None, None),
        P("mp", None, None),
    )

    return jax.shard_map(
        local,
        mesh=mesh,
        in_specs=placed,
        out_specs=(
            P("mp", dp),
            P("mp", dp),
            P("mp", dp, None),
            P("mp", dp, None),
            P("mp", dp, None),
        ),
        check_vma=False,
    )
```

```python
import jax
import jax.numpy as jnp
from jax import lax
from jax.sharding import Mesh
from jax.sharding import PartitionSpec as P


input_scale = 2.0
output_scale = 0.5


def perm_matrix(block_perm):
    count = block_perm.shape[1]
    targets = lax.broadcasted_iota(jnp.int32, (1, 1, count), 2)
    return (block_perm[:, :, None] == targets).astype(jnp.bfloat16)


def own_bits():
    dy = lax.axis_index("dy")
    return (lax.axis_index("core"), dy % 2, lax.axis_index("dz"), dy // 2)


def relabel(x, axis):
    core, dy0, dz, dy1 = own_bits()
    for offset, bit in ((0, dy1), (1, dy0), (2, dz), (3, core)):
        x = jnp.where(bit == 1, jnp.flip(x, axis + offset), x)
    return x


def tree_reduce(acc, order, first, dims=("dy1", "dy0", "dz", "core")):
    n_dy = lax.axis_size("dy")
    swaps = {
        "core": ("core", [(0, 1), (1, 0)]),
        "dy0": ("dy", [(i, i ^ 1) for i in range(n_dy)]),
        "dz": ("dz", [(0, 1), (1, 0)]),
        "dy1": ("dy", [(i, i ^ 2) for i in range(n_dy)]),
    }
    dims = list(dims)
    total = None
    for bit in order:
        axis = first + dims.index(bit)
        dims.remove(bit)
        name, pairs = swaps[bit]
        got = lax.ppermute(lax.index_in_dim(acc, 1, axis, keepdims=False), name, perm=pairs)
        total = lax.index_in_dim(acc, 0, axis, keepdims=False).astype(
            jnp.float32
        ) + got.astype(jnp.float32)
        acc = total.astype(jnp.bfloat16)
    return total


ORDER_A = ("core", "dy0", "dz", "dy1")
ORDER_B = ("core", "dz", "dy0", "dy1")


def local(features, cotangent, block_perm, w_gate, w_up, w_down):
    tok_count = features.shape[1]
    blocks_here = w_gate.shape[0]
    inner = w_gate.shape[1]
    hidden_width = w_gate.shape[2]
    n_mp = lax.axis_size("mp")
    n_dp = lax.axis_size("dy") * lax.axis_size("dz") * lax.axis_size("core")
    block_total = blocks_here * n_mp
    piece = inner // block_total
    s_here = features.shape[0] // (block_total * piece)
    grad_scale = (tok_count * n_dp) ** (-0.5)

    both = jnp.stack([features, cotangent]).reshape(2, s_here, block_total, piece, tok_count)
    both = lax.all_to_all(both, "mp", split_axis=2, concat_axis=1, tiled=True)
    feat_blocks = both[0]
    cot_blocks = both[1]

    onehot = perm_matrix(block_perm)
    feat_rows = feat_blocks.transpose(1, 0, 2, 3).reshape(blocks_here, inner, tok_count)
    feat_p = jnp.einsum(
        "bij,bjt->bit", onehot, feat_rows, preferred_element_type=jnp.float32
    ).astype(jnp.bfloat16)

    gate = (
        jnp.einsum("bit,bih->bth", feat_p, w_gate, preferred_element_type=jnp.float32)
        * input_scale
    )
    up = (
        jnp.einsum("bit,bih->bth", feat_p, w_up, preferred_element_type=jnp.float32)
        * input_scale
    )
    sig = jax.nn.sigmoid(gate)
    act = gate * sig
    hidden = (act * up).astype(jnp.bfloat16)
    down_view = w_down.reshape(blocks_here, hidden_width, block_total, piece)

    n_dy = lax.axis_size("dy")
    cot_rows = cot_blocks.transpose(1, 0, 2, 3).reshape(blocks_here, inner, tok_count)
    n_chunk = 4 * n_dy
    dp_index = (lax.axis_index("dy") * 2 + lax.axis_index("dz")) * 2 + lax.axis_index("core")
    down_nat = (
        jnp.einsum("bth,bjt->bhj", hidden, cot_rows, preferred_element_type=jnp.float32)
        * (output_scale * grad_scale)
    ).astype(jnp.bfloat16)
    down_nat = down_nat.reshape(blocks_here, n_chunk, hidden_width // n_chunk, inner)
    down_part = jnp.stack(
        [lax.dynamic_index_in_dim(down_nat, c ^ dp_index, 1, keepdims=False) for c in range(n_chunk)],
        axis=1,
    ).reshape((blocks_here, n_dy // 2, 2, 2, 2) + down_nat.shape[2:])
    down_grad = jnp.stack(
        [tree_reduce(down_part[b], (ORDER_A, ORDER_B)[b % 2], 0) for b in range(blocks_here)]
    )

    mixed = (
        jnp.einsum("bth,bhsk->sbkt", hidden, down_view, preferred_element_type=jnp.float32)
        * output_scale
    ).astype(jnp.bfloat16)
    outputs = lax.all_to_all(mixed, "mp", split_axis=0, concat_axis=1, tiled=True).reshape(
        features.shape
    )

    d_hidden = (
        jnp.einsum("sbkt,bhsk->bth", cot_blocks, down_view, preferred_element_type=jnp.float32)
        * output_scale
    )
    d_gate = (d_hidden * up * (sig * (1.0 + gate * (1.0 - sig)))).astype(jnp.bfloat16)
    d_up = (d_hidden * act).astype(jnp.bfloat16)

    feat_l = relabel(
        feat_p.reshape(blocks_here, n_dy // 2, 2, 2, 2, inner // (4 * n_dy), tok_count), 1
    )
    d_both = jnp.stack([d_gate, d_up])
    gate_up_part = (
        jnp.einsum(
            "bwyzcrt,gbth->gbwyzcrh", feat_l, d_both, preferred_element_type=jnp.float32
        )
        * (input_scale * grad_scale)
    ).astype(jnp.bfloat16)
    gate_core = tree_reduce(gate_up_part[0], ORDER_A[:1], 1).astype(jnp.bfloat16)
    up_core = tree_reduce(gate_up_part[1], ORDER_B[:1], 1).astype(jnp.bfloat16)
    gate_core, up_core, d_gate, d_up = lax.optimization_barrier((gate_core, up_core, d_gate, d_up))
    rest = ("dy1", "dy0", "dz")
    gate_grad = tree_reduce(gate_core, ORDER_A[1:], 1, rest)
    up_grad = tree_reduce(up_core, ORDER_B[1:], 1, rest)

    d_mixed_p = (
        (
            jnp.einsum("bth,bih->bit", d_gate, w_gate, preferred_element_type=jnp.float32)
            + jnp.einsum("bth,bih->bit", d_up, w_up, preferred_element_type=jnp.float32)
        )
        * input_scale
    ).astype(jnp.bfloat16)
    d_mixed = jnp.einsum(
        "bij,bit->bjt", onehot, d_mixed_p, preferred_element_type=jnp.float32
    ).astype(jnp.bfloat16)
    d_mixed = d_mixed.reshape(blocks_here, block_total, piece, tok_count).transpose(1, 0, 2, 3)

    d_features = lax.all_to_all(d_mixed, "mp", split_axis=0, concat_axis=1, tiled=True).reshape(
        features.shape
    )
    return (outputs, d_features, gate_grad, up_grad, down_grad)


def solution(mesh):
    dp_size = mesh.shape["dp"]
    devices = mesh.devices.reshape(dp_size // 4, 2, 2, mesh.shape["mp"])
    mesh = Mesh(devices, ("dy", "dz", "core", "mp"))
    dp = ("dy", "dz", "core")
    placed = (
        P("mp", dp),
        P("mp", dp),
        P("mp", None),
        P("mp", None, None),
        P("mp", None, None),
        P("mp", None, None),
    )

    return jax.shard_map(
        local,
        mesh=mesh,
        in_specs=placed,
        out_specs=(
            P("mp", dp),
            P("mp", dp),
            P("mp", dp, None),
            P("mp", dp, None),
            P("mp", dp, None),
        ),
        check_vma=False,
    )
```

```python
import jax
import jax.numpy as jnp
from jax import lax
from jax.sharding import Mesh
from jax.sharding import PartitionSpec as P


input_scale = 2.0
output_scale = 0.5


def perm_matrix(block_perm):
    count = block_perm.shape[1]
    targets = lax.broadcasted_iota(jnp.int32, (1, 1, count), 2)
    return (block_perm[:, :, None] == targets).astype(jnp.bfloat16)


def own_bits():
    dy = lax.axis_index("dy")
    return (lax.axis_index("core"), dy % 2, lax.axis_index("dz"), dy // 2)


def relabel(x, axis):
    core, dy0, dz, dy1 = own_bits()
    for offset, bit in ((0, dy1), (1, dy0), (2, dz), (3, core)):
        x = jnp.where(bit == 1, jnp.flip(x, axis + offset), x)
    return x


def tree_reduce(acc, order, first, dims=("dy1", "dy0", "dz", "core")):
    n_dy = lax.axis_size("dy")
    swaps = {
        "core": ("core", [(0, 1), (1, 0)]),
        "dy0": ("dy", [(i, i ^ 1) for i in range(n_dy)]),
        "dz": ("dz", [(0, 1), (1, 0)]),
        "dy1": ("dy", [(i, i ^ 2) for i in range(n_dy)]),
    }
    dims = list(dims)
    total = None
    for bit in order:
        axis = first + dims.index(bit)
        dims.remove(bit)
        name, pairs = swaps[bit]
        got = lax.ppermute(lax.index_in_dim(acc, 1, axis, keepdims=False), name, perm=pairs)
        total = lax.index_in_dim(acc, 0, axis, keepdims=False).astype(
            jnp.float32
        ) + got.astype(jnp.float32)
        acc = total.astype(jnp.bfloat16)
    return total


ORDER_A = ("core", "dy0", "dz", "dy1")
ORDER_B = ("core", "dz", "dy0", "dy1")


def local(features, cotangent, block_perm, w_gate, w_up, w_down):
    tok_count = features.shape[1]
    blocks_here = w_gate.shape[0]
    inner = w_gate.shape[1]
    hidden_width = w_gate.shape[2]
    n_mp = lax.axis_size("mp")
    n_dp = lax.axis_size("dy") * lax.axis_size("dz") * lax.axis_size("core")
    block_total = blocks_here * n_mp
    piece = inner // block_total
    s_here = features.shape[0] // (block_total * piece)
    grad_scale = (tok_count * n_dp) ** (-0.5)

    local_shape = (s_here, block_total, piece, tok_count)
    feat_blocks = lax.all_to_all(
        features.reshape(local_shape), "mp", split_axis=1, concat_axis=0, tiled=True
    )
    cot_blocks = lax.all_to_all(
        cotangent.reshape(local_shape), "mp", split_axis=1, concat_axis=0, tiled=True
    )

    onehot = perm_matrix(block_perm)
    feat_rows = feat_blocks.transpose(1, 0, 2, 3).reshape(blocks_here, inner, tok_count)
    feat_p = jnp.einsum(
        "bij,bjt->bit", onehot, feat_rows, preferred_element_type=jnp.float32
    ).astype(jnp.bfloat16)

    gate = (
        jnp.einsum("bit,bih->bth", feat_p, w_gate, preferred_element_type=jnp.float32)
        * input_scale
    )
    up = (
        jnp.einsum("bit,bih->bth", feat_p, w_up, preferred_element_type=jnp.float32)
        * input_scale
    )
    sig = jax.nn.sigmoid(gate)
    act = gate * sig
    hidden = (act * up).astype(jnp.bfloat16)
    down_view = w_down.reshape(blocks_here, hidden_width, block_total, piece)

    n_dy = lax.axis_size("dy")
    cot_rows = cot_blocks.transpose(1, 0, 2, 3).reshape(blocks_here, inner, tok_count)
    n_chunk = 4 * n_dy
    dp_index = (lax.axis_index("dy") * 2 + lax.axis_index("dz")) * 2 + lax.axis_index("core")
    down_nat = (
        jnp.einsum("bth,bjt->bhj", hidden, cot_rows, preferred_element_type=jnp.float32)
        * (output_scale * grad_scale)
    ).astype(jnp.bfloat16)
    down_nat = down_nat.reshape(blocks_here, n_chunk, hidden_width // n_chunk, inner)
    down_part = jnp.stack(
        [lax.dynamic_index_in_dim(down_nat, c ^ dp_index, 1, keepdims=False) for c in range(n_chunk)],
        axis=1,
    ).reshape((blocks_here, n_dy // 2, 2, 2, 2) + down_nat.shape[2:])
    down_grad = jnp.stack(
        [tree_reduce(down_part[b], (ORDER_A, ORDER_B)[b % 2], 0) for b in range(blocks_here)]
    )

    mixed = (
        jnp.einsum("bth,bhsk->sbkt", hidden, down_view, preferred_element_type=jnp.float32)
        * output_scale
    ).astype(jnp.bfloat16)
    outputs = lax.all_to_all(mixed, "mp", split_axis=0, concat_axis=1, tiled=True).reshape(
        features.shape
    )

    d_hidden = (
        jnp.einsum("sbkt,bhsk->bth", cot_blocks, down_view, preferred_element_type=jnp.float32)
        * output_scale
    )
    d_gate = (d_hidden * up * (sig * (1.0 + gate * (1.0 - sig)))).astype(jnp.bfloat16)
    d_up = (d_hidden * act).astype(jnp.bfloat16)

    feat_l = relabel(
        feat_p.reshape(blocks_here, n_dy // 2, 2, 2, 2, inner // (4 * n_dy), tok_count), 1
    )
    d_both = jnp.stack([d_gate, d_up])
    gate_up_part = (
        jnp.einsum(
            "bwyzcrt,gbth->gbwyzcrh", feat_l, d_both, preferred_element_type=jnp.float32
        )
        * (input_scale * grad_scale)
    ).astype(jnp.bfloat16)
    gate_core = tree_reduce(gate_up_part[0], ORDER_A[:1], 1).astype(jnp.bfloat16)
    up_core = tree_reduce(gate_up_part[1], ORDER_B[:1], 1).astype(jnp.bfloat16)
    gate_core, up_core, d_gate, d_up = lax.optimization_barrier((gate_core, up_core, d_gate, d_up))
    rest = ("dy1", "dy0", "dz")
    gate_grad = tree_reduce(gate_core, ORDER_A[1:], 1, rest)
    up_grad = tree_reduce(up_core, ORDER_B[1:], 1, rest)

    d_mixed_p = (
        (
            jnp.einsum("bth,bih->bit", d_gate, w_gate, preferred_element_type=jnp.float32)
            + jnp.einsum("bth,bih->bit", d_up, w_up, preferred_element_type=jnp.float32)
        )
        * input_scale
    ).astype(jnp.bfloat16)
    d_mixed = jnp.einsum(
        "bij,bit->bjt", onehot, d_mixed_p, preferred_element_type=jnp.float32
    ).astype(jnp.bfloat16)
    d_mixed = d_mixed.reshape(blocks_here, block_total, piece, tok_count).transpose(1, 0, 2, 3)

    d_features = lax.all_to_all(
        d_mixed, "mp", split_axis=0, concat_axis=1, tiled=True
    ).reshape(features.shape)
    return (outputs, d_features, gate_grad, up_grad, down_grad)


def solution(mesh):
    dp_size = mesh.shape["dp"]
    devices = mesh.devices.reshape(dp_size // 4, 2, 2, mesh.shape["mp"])
    mesh = Mesh(devices, ("dy", "dz", "core", "mp"))
    dp = ("dy", "dz", "core")
    placed = (
        P("mp", dp),
        P("mp", dp),
        P("mp", None),
        P("mp", None, None),
        P("mp", None, None),
        P("mp", None, None),
    )

    return jax.shard_map(
        local,
        mesh=mesh,
        in_specs=placed,
        out_specs=(
            P("mp", dp),
            P("mp", dp),
            P("mp", dp, None),
            P("mp", dp, None),
            P("mp", dp, None),
        ),
        check_vma=False,
    )
```

```python
import jax
import jax.numpy as jnp
from jax import lax
from jax.sharding import Mesh
from jax.sharding import PartitionSpec as P


input_scale = 2.0
output_scale = 0.5


def perm_matrix(block_perm):
    count = block_perm.shape[1]
    targets = lax.broadcasted_iota(jnp.int32, (1, 1, count), 2)
    return (block_perm[:, :, None] == targets).astype(jnp.bfloat16)


def own_bits():
    dy = lax.axis_index("dy")
    return (lax.axis_index("core"), dy % 2, lax.axis_index("dz"), dy // 2)


def relabel(x, axis):
    core, dy0, dz, dy1 = own_bits()
    for offset, bit in ((0, dy1), (1, dy0), (2, dz), (3, core)):
        x = jnp.where(bit == 1, jnp.flip(x, axis + offset), x)
    return x


def tree_reduce(acc, order, first, dims=("dy1", "dy0", "dz", "core")):
    n_dy = lax.axis_size("dy")
    swaps = {
        "core": ("core", [(0, 1), (1, 0)]),
        "dy0": ("dy", [(i, i ^ 1) for i in range(n_dy)]),
        "dz": ("dz", [(0, 1), (1, 0)]),
        "dy1": ("dy", [(i, i ^ 2) for i in range(n_dy)]),
    }
    dims = list(dims)
    total = None
    for bit in order:
        axis = first + dims.index(bit)
        dims.remove(bit)
        name, pairs = swaps[bit]
        got = lax.ppermute(lax.index_in_dim(acc, 1, axis, keepdims=False), name, perm=pairs)
        total = lax.index_in_dim(acc, 0, axis, keepdims=False).astype(
            jnp.float32
        ) + got.astype(jnp.float32)
        acc = total.astype(jnp.bfloat16)
    return total


ORDER_A = ("core", "dy0", "dz", "dy1")
ORDER_B = ("core", "dz", "dy0", "dy1")


def local(features, cotangent, block_perm, w_gate, w_up, w_down):
    tok_count = features.shape[1]
    blocks_here = w_gate.shape[0]
    inner = w_gate.shape[1]
    hidden_width = w_gate.shape[2]
    n_mp = lax.axis_size("mp")
    n_dp = lax.axis_size("dy") * lax.axis_size("dz") * lax.axis_size("core")
    block_total = blocks_here * n_mp
    piece = inner // block_total
    s_here = features.shape[0] // (block_total * piece)
    grad_scale = (tok_count * n_dp) ** (-0.5)

    local_shape = (s_here, block_total, piece, tok_count)
    feat_blocks = lax.all_to_all(
        features.reshape(local_shape), "mp", split_axis=1, concat_axis=0, tiled=True
    )
    cot_blocks = lax.all_to_all(
        cotangent.reshape(local_shape), "mp", split_axis=1, concat_axis=0, tiled=True
    )

    onehot = perm_matrix(block_perm)
    feat_rows = feat_blocks.transpose(1, 0, 2, 3).reshape(blocks_here, inner, tok_count)
    feat_p = jnp.einsum(
        "bij,bjt->bit", onehot, feat_rows, preferred_element_type=jnp.float32
    ).astype(jnp.bfloat16)

    gate = (
        jnp.einsum("bit,bih->bth", feat_p, w_gate, preferred_element_type=jnp.float32)
        * input_scale
    )
    up = (
        jnp.einsum("bit,bih->bth", feat_p, w_up, preferred_element_type=jnp.float32)
        * input_scale
    )
    sig = jax.nn.sigmoid(gate)
    act = gate * sig
    hidden = (act * up).astype(jnp.bfloat16)
    down_view = w_down.reshape(blocks_here, hidden_width, block_total, piece)

    n_dy = lax.axis_size("dy")
    cot_rows = cot_blocks.transpose(1, 0, 2, 3).reshape(blocks_here, inner, tok_count)
    n_chunk = 4 * n_dy
    dp_index = (lax.axis_index("dy") * 2 + lax.axis_index("dz")) * 2 + lax.axis_index("core")
    down_nat = (
        jnp.einsum("bth,bjt->bhj", hidden, cot_rows, preferred_element_type=jnp.float32)
        * (output_scale * grad_scale)
    ).astype(jnp.bfloat16)
    down_nat = down_nat.reshape(blocks_here, n_chunk, hidden_width // n_chunk, inner)
    down_part = jnp.stack(
        [lax.dynamic_index_in_dim(down_nat, c ^ dp_index, 1, keepdims=False) for c in range(n_chunk)],
        axis=1,
    ).reshape((blocks_here, n_dy // 2, 2, 2, 2) + down_nat.shape[2:])
    down_grad = jnp.stack(
        [tree_reduce(down_part[b], (ORDER_A, ORDER_B)[b % 2], 0) for b in range(blocks_here)]
    )

    mixed = (
        jnp.einsum("bth,bhsk->sbkt", hidden, down_view, preferred_element_type=jnp.float32)
        * output_scale
    ).astype(jnp.bfloat16)
    outputs = lax.all_to_all(mixed, "mp", split_axis=0, concat_axis=1, tiled=True).reshape(
        features.shape
    )

    d_hidden = (
        jnp.einsum("sbkt,bhsk->bth", cot_blocks, down_view, preferred_element_type=jnp.float32)
        * output_scale
    )
    d_gate = (d_hidden * up * (sig * (1.0 + gate * (1.0 - sig)))).astype(jnp.bfloat16)
    d_up = (d_hidden * act).astype(jnp.bfloat16)

    feat_l = relabel(
        feat_p.reshape(blocks_here, n_dy // 2, 2, 2, 2, inner // (4 * n_dy), tok_count), 1
    )
    d_both = jnp.stack([d_gate, d_up])
    gate_up_part = (
        jnp.einsum(
            "bwyzcrt,gbth->gbwyzcrh", feat_l, d_both, preferred_element_type=jnp.float32
        )
        * (input_scale * grad_scale)
    ).astype(jnp.bfloat16)
    gate_core = tree_reduce(gate_up_part[0], ORDER_A[:1], 1).astype(jnp.bfloat16)
    up_core = tree_reduce(gate_up_part[1], ORDER_B[:1], 1).astype(jnp.bfloat16)
    rest = ("dy1", "dy0", "dz")
    gate_grad = tree_reduce(gate_core, ORDER_A[1:], 1, rest)
    up_grad = tree_reduce(up_core, ORDER_B[1:], 1, rest)

    d_mixed_p = (
        (
            jnp.einsum("bth,bih->bit", d_gate, w_gate, preferred_element_type=jnp.float32)
            + jnp.einsum("bth,bih->bit", d_up, w_up, preferred_element_type=jnp.float32)
        )
        * input_scale
    ).astype(jnp.bfloat16)
    d_mixed = jnp.einsum(
        "bij,bit->bjt", onehot, d_mixed_p, preferred_element_type=jnp.float32
    ).astype(jnp.bfloat16)
    d_mixed = d_mixed.reshape(blocks_here, block_total, piece, tok_count).transpose(1, 0, 2, 3)

    d_features = lax.all_to_all(d_mixed, "mp", split_axis=0, concat_axis=1, tiled=True).reshape(
        features.shape
    )
    return (outputs, d_features, gate_grad, up_grad, down_grad)


def solution(mesh):
    dp_size = mesh.shape["dp"]
    devices = mesh.devices.reshape(dp_size // 4, 2, 2, mesh.shape["mp"])
    mesh = Mesh(devices, ("dy", "dz", "core", "mp"))
    dp = ("dy", "dz", "core")
    placed = (
        P("mp", dp),
        P("mp", dp),
        P("mp", None),
        P("mp", None, None),
        P("mp", None, None),
        P("mp", None, None),
    )

    return jax.shard_map(
        local,
        mesh=mesh,
        in_specs=placed,
        out_specs=(
            P("mp", dp),
            P("mp", dp),
            P("mp", dp, None),
            P("mp", dp, None),
            P("mp", dp, None),
        ),
        check_vma=False,
    )
```
